512 devices in a mesh: req: 64 (over x, z, core), mdl: 8 (over y).
Axes of the slice: x: 4, y: 8, z: 8, core: 2. Of those that a mesh axis runs over, the one named last changes fastest.
Arguments:
- queries: bfloat16 [1536, 2048], P('req', 'mdl'), may hold values from -6 to 6
- scored_key_value: bfloat16 [2, 1536, 1024], P(None, 'req', 'mdl'), may hold values from -6 to 6
- gate_logits: bfloat16 [1536, 2048], P('req', 'mdl'), may hold values from -8 to 8
- page_kv: bfloat16 [2, 2176, 128, 1024], P(None, 'req', None, 'mdl'), may hold values from -6 to 6
- page_table: int32 [64, 128], replicated, may hold values from -1 to 2175, as said below
- lengths: int32 [64], replicated, may hold values from 1 to 16384
- assignment: int32 [64], replicated, may hold values from 0 to 63, each once
- offsets: int32 [64, 24], P('req'), may hold values from 0 to 23, each once within a row
- residual: bfloat16 [1536, 2048], P('req'), may hold values from -18 to 18
- out_weight: bfloat16 [2048, 2048], P('mdl'), may hold values from -1 to 1
- norm_gain: bfloat16 [2048], replicated, may hold values from 0.5 to 1.5
- head_weight: bfloat16 [2048, 131072], P(None, ('req', 'mdl')), may hold values from -0.3193592 to 0.3193592
- targets: int32 [1536], replicated, may hold values from 0 to 131071
Outputs:
- logprob: float32 [1536], P('req')
- entropy: float32 [1536], P('req')
The draws below stay inside these ranges and needn't reach their ends.
Inputs may be any that keep to these rules, and one draw needn't show every extreme that they name: `page_table`: row i lists the pages of request i in order, each as owner index times 34 plus a slot, followed by -1. Request i has ceil(lengths[i] / 128) pages, no page serves two requests, and at most 2 pages of one request sit on one owner. `assignment`: each index along req holds exactly one request. `offsets`: each row is an order of 0 to 23.
All inputs are finite; a program needn't handle non-finite values.
Results may differ from the reference program's by a relative error of at most 0.0013.
Values may be sent and summed in bfloat16 or wider, within the bound.
No kernel may reach another device: no remote copies, remote signals or barrier semaphores. Data moves between devices by JAX's collectives and lax.ppermute only.
A program may use at most 128 MiB of HBM per device.

```python
import math
import jax
import jax.numpy as jnp
import numpy as np
from jax import lax

D = 2048
QUERY_HEADS = 16
KEY_VALUE_HEADS = 8
HEAD_SIZE = 128
PAGE_TOKENS = 128
CAP = 2
REQUEST_TOKENS = 24
NREQ = 64
TOTAL_TOKENS = 1536
PAGES_DEV = 34
TOTAL_PAGES = 2176
REQUEST_PAGES = 128
VOCAB = 131072


def pages_layout(key):
    subkeys = jax.random.split(jax.random.fold_in(key, 11), 5)
    half_count = NREQ // 2
    pair_count = (NREQ - 2) // 2
    pair_shift = jax.random.randint(subkeys[0], (pair_count,), 1 - half_count, half_count)
    paired = jnp.stack([half_count + pair_shift, half_count - pair_shift], axis=1).reshape(-1)
    others = jnp.concatenate([paired, jnp.full((1,), half_count, jnp.int32)]).astype(jnp.int32)
    counts = jnp.concatenate([others, jnp.full((1,), REQUEST_PAGES, jnp.int32)]).astype(jnp.int32)
    starts = jnp.concatenate([jnp.zeros((1,), jnp.int32), jnp.cumsum(others).astype(jnp.int32)])
    page_index = jnp.arange(REQUEST_PAGES, dtype=jnp.int32)[None, :]
    sequence = starts[:, None] + page_index
    is_long = (jnp.arange(NREQ, dtype=jnp.int32) == NREQ - 1)[:, None]
    page_owner = jnp.where(is_long, page_index % NREQ, sequence % NREQ)
    page_slot = jnp.where(is_long, page_index // NREQ, CAP + sequence // NREQ)
    owner_perm = jax.random.permutation(subkeys[1], NREQ).astype(jnp.int32)
    slot_perm = jax.random.permutation(subkeys[2], PAGES_DEV).astype(jnp.int32)
    global_ids = owner_perm[page_owner] * PAGES_DEV + slot_perm[jnp.minimum(page_slot, PAGES_DEV - 1)]
    page_rows = jnp.where(page_index < counts[:, None], global_ids, -1)
    last_fill = jax.random.randint(subkeys[3], (NREQ,), 1, PAGE_TOKENS + 1)
    cached = (counts - 1) * PAGE_TOKENS + jnp.where(is_long[:, 0], PAGE_TOKENS, last_fill)
    id_order = jax.random.permutation(subkeys[4], NREQ).astype(jnp.int32)
    inverse = jnp.argsort(id_order)
    return (page_rows[inverse].astype(jnp.int32), cached[inverse].astype(jnp.int32))


def draw_page_table(key, part):
    return pages_layout(key)[0]


def draw_lengths(key, part):
    return pages_layout(key)[1]


def head_sign_flips(key):
    random_bits = jax.random.randint(jax.random.fold_in(key, 29), (KEY_VALUE_HEADS, HEAD_SIZE), 0, 2)
    return (2 * random_bits - 1).astype(jnp.float32)


def ungated_rows(key, shape):
    return jnp.clip(jax.random.normal(key, shape, jnp.float32), -6.0, 6.0)


def drawn_rows(key, token_rows, sign_flips):
    subkeys = jax.random.split(key, 1)
    heads = sign_flips.shape[0]
    base = ungated_rows(subkeys[0], (token_rows, heads, HEAD_SIZE))
    return base


def draw_queries(key, part):
    sign_flips = jnp.repeat(head_sign_flips(key), QUERY_HEADS // KEY_VALUE_HEADS, axis=0)
    values = drawn_rows(jax.random.fold_in(key, 31), TOTAL_TOKENS, sign_flips)
    return values.reshape(TOTAL_TOKENS, QUERY_HEADS * HEAD_SIZE).astype(jnp.bfloat16)


def draw_scored_key_value(key, part):
    key_portion = drawn_rows(jax.random.fold_in(key, 51), TOTAL_TOKENS, head_sign_flips(key))
    value_portion = ungated_rows(jax.random.fold_in(key, 52), (TOTAL_TOKENS, KEY_VALUE_HEADS, HEAD_SIZE))
    return jnp.stack([key_portion.reshape(TOTAL_TOKENS, KEY_VALUE_HEADS * HEAD_SIZE), value_portion.reshape(TOTAL_TOKENS, KEY_VALUE_HEADS * HEAD_SIZE)]).astype(jnp.bfloat16)


def draw_page_kv(key, part):
    token_rows = TOTAL_PAGES * PAGE_TOKENS
    key_portion = drawn_rows(jax.random.fold_in(key, 53), token_rows, head_sign_flips(key))
    value_portion = ungated_rows(jax.random.fold_in(key, 54), (token_rows, KEY_VALUE_HEADS, HEAD_SIZE))
    stacked_pair = jnp.stack([key_portion.reshape(TOTAL_PAGES, PAGE_TOKENS, KEY_VALUE_HEADS * HEAD_SIZE), value_portion.reshape(TOTAL_PAGES, PAGE_TOKENS, KEY_VALUE_HEADS * HEAD_SIZE)])
    return stacked_pair.astype(jnp.bfloat16)


def draw_residual(key, part):
    subkeys = jax.random.split(jax.random.fold_in(key, 61), 3)
    row_scale = jnp.exp(jax.random.uniform(subkeys[0], (TOTAL_TOKENS, 1), jnp.float32, jnp.log(0.1), jnp.log(1.0)))
    col_scale = jnp.exp(jax.random.uniform(subkeys[1], (1, D), jnp.float32, jnp.log(0.3), jnp.log(3.0)))
    values = jnp.clip(jax.random.normal(subkeys[2], (TOTAL_TOKENS, D), jnp.float32), -6.0, 6.0) * row_scale * col_scale
    return values.astype(jnp.bfloat16)


def draw_head_weight(key, part):
    subkeys = jax.random.split(jax.random.fold_in(key, 71), 1)
    spread = (1.5 + 2.0 * jnp.arange(VOCAB, dtype=jnp.float32)[None, :] / VOCAB) * D ** (-0.5)
    values = jnp.clip(jax.random.normal(subkeys[0], (D, VOCAB), jnp.float32), -4.0, 4.0) * spread
    return values.astype(jnp.bfloat16)


def plant(entries, key, low, largest):
    longest = entries.shape.index(max(entries.shape))
    spots = []
    for shift in (0, 1):
        where = [jax.random.randint(jax.random.fold_in(key, axis), (), 0, length) for axis, length in enumerate(entries.shape)]
        where[longest] = (where[longest] + shift) % entries.shape[longest]
        spots.append(tuple(where))
    return entries.at[spots[0]].set(low).at[spots[1]].set(largest)


def block_scale(stream_key, extent, cuts, smallest, largest):
    def one(position, parts):
        draws = jax.random.uniform(jax.random.fold_in(jax.random.fold_in(stream_key, 6), position), (parts,), jnp.float32, smallest / len(cuts), largest / len(cuts))
        return jnp.repeat(jnp.exp(draws), extent[position] // parts).reshape((-1,) + (1,) * (len(extent) - position - 1))

    loudness = one(*cuts[0])
    for cut in cuts[1:]:
        loudness = loudness * one(*cut)
    return loudness


def skewed_wide(key, shape, amount, slope):
    weights = [min(1 << octave, amount + 1 - (1 << octave)) * (1 << 20) // math.isqrt((1 << octave) ** slope) + 1 for octave in range((amount + 1).bit_length()) if 1 << octave <= amount]
    deviation = 1 + sum(weights) // (1 << 30)
    grid = np.cumsum(np.array([max(1, weight // deviation) for weight in weights]))
    lot = jax.random.randint(jax.random.fold_in(key, 1), shape, 0, int(grid[len(weights) - 1]))
    start = jnp.left_shift(1, jnp.searchsorted(jnp.asarray(grid, jnp.int32), lot, side="right").astype(jnp.int32))
    standing = start - 1 + jax.random.randint(jax.random.fold_in(key, 4), shape, 0, 1 << 30) % jnp.minimum(start, amount + 1 - start)
    return jax.random.permutation(jax.random.fold_in(key, 2), amount)[standing].astype(jnp.int32)


def gaussian(rng, dims, deviation, bound, shards=(), kind=jnp.bfloat16):
    result = deviation * jax.random.normal(rng, dims, jnp.float32)
    if shards:
        result = result * block_scale(rng, dims, shards, -0.22, 0.18)
    return jnp.clip(result, -bound, bound).astype(kind)


def setup_inputs(seed: int = 0) -> dict:
    key_of = jax.random.split(jax.random.key(seed), 14)
    queries = draw_queries(jax.random.fold_in(key_of[13], 71), 0)
    scored_key_value = draw_scored_key_value(jax.random.fold_in(key_of[13], 71), 0)
    gate_logits = gaussian(key_of[2], (TOTAL_TOKENS, QUERY_HEADS * HEAD_SIZE), 2.0, 8.0, ((0, 64), (1, 8)))
    page_kv = draw_page_kv(jax.random.fold_in(key_of[13], 71), 0)
    page_table = draw_page_table(jax.random.fold_in(key_of[13], 71), 0)
    lengths = draw_lengths(jax.random.fold_in(key_of[13], 71), 0)
    assignment = jax.random.permutation(key_of[6], NREQ).astype(jnp.int32)
    offsets = jax.vmap(lambda own: jax.random.permutation(own, REQUEST_TOKENS))(jax.random.split(key_of[7], NREQ)).reshape((NREQ, REQUEST_TOKENS)).astype(jnp.int32)
    residual = draw_residual(jax.random.fold_in(key_of[13], 71), 0)
    out_weight = gaussian(key_of[9], (QUERY_HEADS * HEAD_SIZE, D), 0.066, 1.0, ((0, 8),))
    norm_gain = jnp.clip(1.0 + 0.1 * jax.random.normal(key_of[10], (D,), jnp.float32), 0.5, 1.5).astype(jnp.bfloat16)
    head_weight = draw_head_weight(jax.random.fold_in(key_of[13], 71), 0)
    targets = plant(skewed_wide(key_of[12], (TOTAL_TOKENS,), VOCAB, 2), jax.random.fold_in(key_of[12], 3), 0, VOCAB - 1).astype(jnp.int32)
    return {"queries": queries, "scored_key_value": scored_key_value, "gate_logits": gate_logits, "page_kv": page_kv, "page_table": page_table, "lengths": lengths, "assignment": assignment, "offsets": offsets, "residual": residual, "out_weight": out_weight, "norm_gain": norm_gain, "head_weight": head_weight, "targets": targets}


FLOOR_SCORE = -1e+30
NORM_EPSILON = 1e-06

def reference(queries, scored_key_value, gate_logits, page_kv, page_table, lengths, assignment, offsets, residual, out_weight, norm_gain, head_weight, targets):
    queries_per_group = QUERY_HEADS // KEY_VALUE_HEADS
    score_scale = HEAD_SIZE ** (-0.5)
    indices = jnp.arange(NREQ, dtype=jnp.int32)
    holder = lax.optimization_barrier(jnp.sum(jnp.where(assignment[:, None] == indices[None, :], indices[:, None], 0), axis=0)).astype(jnp.int32)
    paged_key_store = page_kv[0]
    paged_value_store = page_kv[1]
    positions = jnp.arange(REQUEST_PAGES * PAGE_TOKENS, dtype=jnp.int32)

    def one_request(device):
        request = holder[device]
        page_table_row = jnp.maximum(page_table[request], 0).astype(jnp.int32)
        length = lengths[request]
        joined_keys = jnp.take(paged_key_store, page_table_row, axis=0).reshape(REQUEST_PAGES * PAGE_TOKENS, KEY_VALUE_HEADS, HEAD_SIZE).astype(jnp.float32)
        joined_values = jnp.take(paged_value_store, page_table_row, axis=0).reshape(REQUEST_PAGES * PAGE_TOKENS, KEY_VALUE_HEADS, HEAD_SIZE).astype(jnp.float32)
        first_row = (device * REQUEST_TOKENS).astype(jnp.int32)
        query_matrix = lax.dynamic_slice_in_dim(queries, first_row, REQUEST_TOKENS, 0).reshape(REQUEST_TOKENS, KEY_VALUE_HEADS, queries_per_group, HEAD_SIZE).astype(jnp.float32)
        scored_keys = lax.dynamic_slice_in_dim(scored_key_value[0], first_row, REQUEST_TOKENS, 0).reshape(REQUEST_TOKENS, KEY_VALUE_HEADS, HEAD_SIZE).astype(jnp.float32)
        scored_values = lax.dynamic_slice_in_dim(scored_key_value[1], first_row, REQUEST_TOKENS, 0).reshape(REQUEST_TOKENS, KEY_VALUE_HEADS, HEAD_SIZE).astype(jnp.float32)
        gate_rows = lax.dynamic_slice_in_dim(gate_logits, first_row, REQUEST_TOKENS, 0).astype(jnp.float32)
        fresh_order = offsets[device]
        old_scores = jnp.einsum('tjgd,ljd->jgtl', query_matrix, joined_keys) * score_scale
        old_scores = jnp.where(positions < length, old_scores, FLOOR_SCORE)
        new_scores = jnp.einsum('tjgd,ujd->jgtu', query_matrix, scored_keys) * score_scale
        new_scores = jnp.where(fresh_order[None, :] <= fresh_order[:, None], new_scores, FLOOR_SCORE)
        row_top = jnp.maximum(lax.optimization_barrier(jnp.max(old_scores, axis=-1)), lax.optimization_barrier(jnp.max(new_scores, axis=-1)))
        old_weights = jnp.exp(old_scores - row_top[..., None])
        new_weights = jnp.exp(new_scores - row_top[..., None])
        weight_sum = lax.optimization_barrier(jnp.sum(old_weights, axis=-1)) + lax.optimization_barrier(jnp.sum(new_weights, axis=-1))
        old_rounded = lax.optimization_barrier(old_weights.astype(jnp.bfloat16)).astype(jnp.float32)
        new_rounded = lax.optimization_barrier(new_weights.astype(jnp.bfloat16)).astype(jnp.float32)
        summed = jnp.einsum('jgtl,ljd->tjgd', old_rounded, joined_values) + jnp.einsum('jgtu,ujd->tjgd', new_rounded, scored_values)
        attended = summed / jnp.transpose(weight_sum, (2, 0, 1))[..., None]
        return (attended.reshape(REQUEST_TOKENS, QUERY_HEADS * HEAD_SIZE) * jax.nn.sigmoid(gate_rows)).astype(jnp.bfloat16)
    gated_out = lax.map(one_request, indices).reshape(TOTAL_TOKENS, QUERY_HEADS * HEAD_SIZE)
    update = jnp.dot(gated_out, out_weight, preferred_element_type=jnp.float32)
    stream = residual.astype(jnp.float32) + update
    normed = (stream * lax.rsqrt(lax.optimization_barrier(jnp.mean(stream * stream, axis=-1, keepdims=True)) + NORM_EPSILON) * norm_gain.astype(jnp.float32)).astype(jnp.bfloat16)

    def score_rows(block):
        rows_block, target_block = block
        logits = jnp.dot(rows_block, head_weight, preferred_element_type=jnp.float32)
        row_peak = lax.optimization_barrier(jnp.max(logits, axis=-1))
        vocab_weights = jnp.exp(logits - row_peak[:, None])
        vocab_total = lax.optimization_barrier(jnp.sum(vocab_weights, axis=-1))
        moment = lax.optimization_barrier(jnp.sum(vocab_weights * logits, axis=-1))
        chosen = jnp.take_along_axis(logits, target_block[:, None].astype(jnp.int32), axis=1)[:, 0]
        log_total = row_peak + jnp.log(vocab_total)
        return (chosen - log_total, log_total - moment / vocab_total)
    logprob, entropy = lax.map(score_rows, (normed.reshape(NREQ, REQUEST_TOKENS, D), targets.reshape(NREQ, REQUEST_TOKENS)))
    return (logprob.reshape(TOTAL_TOKENS), entropy.reshape(TOTAL_TOKENS))
```

```python
import jax
import jax.numpy as jnp
from jax import lax
from jax.sharding import PartitionSpec as P

HEAD_SIZE = 128
CAP = 2


FLOOR_SCORE = -1e30
NORM_EPSILON = 1e-06


def merge_stats(parts):
    peak = jnp.max(parts[:, :, 0], axis=0)
    scale = jnp.exp(parts[:, :, 0] - peak[None])
    total = jnp.sum(parts[:, :, 1] * scale, axis=0)
    moment = jnp.sum(parts[:, :, 2] * scale, axis=0)
    chosen = jnp.sum(parts[:, :, 3], axis=0)
    return jnp.stack([peak, total, moment, chosen], axis=1)


def body(
    queries,
    scored_key_value,
    gate_logits,
    page_kv,
    page_table,
    lengths,
    assignment,
    offsets,
    residual,
    out_weight,
    norm_gain,
    head_weight,
    targets,
):
    groups = lax.axis_size("req")
    req_index = lax.axis_index("req")
    fresh_count = queries.shape[0]
    kv_heads = scored_key_value.shape[2] // HEAD_SIZE
    queries_per_group = queries.shape[1] // scored_key_value.shape[2]
    page_len = page_kv.shape[2]
    store_pages = page_kv.shape[1]
    page_slots = page_table.shape[1]
    score_scale = HEAD_SIZE ** (-0.5)
    indices = jnp.arange(groups, dtype=jnp.int32)
    holder = jnp.sum(
        jnp.where(assignment[:, None] == indices[None, :], indices[:, None], 0), axis=0
    )
    query_heads = queries.reshape(fresh_count, kv_heads, queries_per_group, HEAD_SIZE)
    scored_keys = scored_key_value[0].reshape(fresh_count, kv_heads, HEAD_SIZE)
    scored_values = scored_key_value[1].reshape(fresh_count, kv_heads, HEAD_SIZE)
    fresh_order = offsets[0]
    visible = fresh_order[None, :] <= fresh_order[:, None]
    fresh_scores = (
        jnp.einsum("tjgd,ujd->jgtu", query_heads, scored_keys, preferred_element_type=jnp.float32)
        * score_scale
    )
    fresh_scores = jnp.where(visible[None, None], fresh_scores, FLOOR_SCORE)
    fresh_top = jnp.max(fresh_scores, axis=-1)
    page_owner = jnp.where(page_table >= 0, page_table // store_pages, -1)
    page_slot = page_table % store_pages
    is_mine = page_owner == req_index
    page_rank = jnp.cumsum(is_mine.astype(jnp.int32), axis=1) - 1
    slot_picks = [
        jnp.sum(jnp.where(is_mine & (page_rank == cap_index), page_slot, 0), axis=1)
        for cap_index in range(CAP)
    ]
    send_slot = jnp.take(jnp.stack(slot_picks, axis=1), holder, axis=0).reshape(-1)
    outgoing = jnp.take(page_kv, send_slot, axis=1)
    arrived = lax.all_to_all(outgoing, "req", split_axis=1, concat_axis=1, tiled=True)
    request = holder[req_index]
    page_table_row = jnp.take(page_table, request, axis=0)
    length = jnp.take(lengths, request)
    row_owner = jnp.where(page_table_row >= 0, page_table_row // store_pages, -1)
    source = row_owner[None, :] == indices[:, None]
    row_rank = jnp.cumsum(source.astype(jnp.int32), axis=1) - 1
    page_fill = jnp.clip(length - jnp.arange(page_slots, dtype=jnp.int32) * page_len, 0, page_len)
    counts = jnp.stack(
        [
            jnp.sum(jnp.where(source & (row_rank == cap_index), page_fill[None, :], 0), axis=1)
            for cap_index in range(CAP)
        ],
        axis=1,
    ).reshape(-1)
    live_keys = (jnp.arange(page_len, dtype=jnp.int32)[None, :] < counts[:, None]).reshape(-1)
    cached_keys = arrived[0].reshape(-1, kv_heads, HEAD_SIZE)
    cached_values = arrived[1].reshape(-1, kv_heads, HEAD_SIZE)
    scores = (
        jnp.einsum("tjgd,ljd->jgtl", query_heads, cached_keys, preferred_element_type=jnp.float32)
        * score_scale
    )
    scores = jnp.where(live_keys[None, None, None, :], scores, FLOOR_SCORE)
    row_top = jnp.maximum(jnp.max(scores, axis=-1), fresh_top)
    weights = jnp.exp(scores - row_top[..., None])
    weight_sum = jnp.sum(weights, axis=-1)
    summed = jnp.einsum(
        "jgtl,ljd->tjgd",
        weights.astype(jnp.bfloat16),
        cached_values,
        preferred_element_type=jnp.float32,
    )
    fresh_weights = jnp.exp(fresh_scores - row_top[..., None])
    weight_sum = weight_sum + jnp.sum(fresh_weights, axis=-1)
    summed = summed + jnp.einsum(
        "jgtu,ujd->tjgd",
        fresh_weights.astype(jnp.bfloat16),
        scored_values,
        preferred_element_type=jnp.float32,
    )
    attended = summed / jnp.transpose(weight_sum, (2, 0, 1))[..., None]
    gated_out = (
        attended.reshape(fresh_count, -1) * jax.nn.sigmoid(gate_logits.astype(jnp.float32))
    ).astype(jnp.bfloat16)
    update = lax.psum(jnp.dot(gated_out, out_weight, preferred_element_type=jnp.float32), "mdl")
    stream = residual.astype(jnp.float32) + update
    normed = (
        stream
        * lax.rsqrt(jnp.mean(stream * stream, axis=-1, keepdims=True) + NORM_EPSILON)
        * norm_gain.astype(jnp.float32)
    ).astype(jnp.bfloat16)
    logits = jnp.dot(
        lax.all_gather(normed, "req", axis=0, tiled=True),
        head_weight,
        preferred_element_type=jnp.float32,
    )
    vocab_width = head_weight.shape[1]
    mdl_size = lax.axis_size("mdl")
    mdl_index = lax.axis_index("mdl")
    vocab_start = (req_index * mdl_size + mdl_index) * vocab_width
    columns = vocab_start + jnp.arange(vocab_width, dtype=jnp.int32)
    chosen = jnp.sum(jnp.where(targets[:, None] == columns[None, :], logits, 0.0), axis=1)
    local_peak = jnp.max(logits, axis=1)
    local_weights = jnp.exp(logits - local_peak[:, None])
    stats = jnp.stack(
        [
            local_peak,
            jnp.sum(local_weights, axis=1),
            jnp.sum(local_weights * logits, axis=1),
            chosen,
        ],
        axis=1,
    ).reshape(groups, fresh_count, 4)
    stats = lax.all_to_all(stats, "req", 0, 0, tiled=True)
    stats = merge_stats(stats)
    slots = jnp.where(
        (jnp.arange(mdl_size, dtype=jnp.int32) == mdl_index)[:, None, None], stats[None], 0.0
    )
    stats = merge_stats(lax.psum(slots, "mdl"))
    row_peak, vocab_total, moment, chosen = (stats[:, i] for i in range(4))
    log_total = row_peak + jnp.log(vocab_total)
    logprob = chosen - log_total
    entropy = log_total - moment / vocab_total
    return (logprob, entropy)


def solution(mesh):
    placed = (
        P("req", "mdl"),
        P(None, "req", "mdl"),
        P("req", "mdl"),
        P(None, "req", None, "mdl"),
        P(),
        P(),
        P(),
        P("req", None),
        P("req", None),
        P("mdl", None),
        P(),
        P(None, ("req", "mdl")),
        P(),
    )
    return jax.shard_map(
        body, mesh=mesh, in_specs=placed, out_specs=(P("req"), P("req")), check_vma=False
    )
```

```python
import jax
import jax.numpy as jnp
from jax import lax
from jax.sharding import PartitionSpec as P

HEAD_SIZE = 128
CAP = 2


FLOOR_SCORE = -1e30
NORM_EPSILON = 1e-06


def merge_stats(parts):
    peak = jnp.max(parts[:, :, 0], axis=0)
    scale = jnp.exp(parts[:, :, 0] - peak[None])
    total = jnp.sum(parts[:, :, 1] * scale, axis=0)
    moment = jnp.sum(parts[:, :, 2] * scale, axis=0)
    chosen = jnp.sum(parts[:, :, 3], axis=0)
    return jnp.stack([peak, total, moment, chosen], axis=1)


def body(
    queries,
    scored_key_value,
    gate_logits,
    page_kv,
    page_table,
    lengths,
    assignment,
    offsets,
    residual,
    out_weight,
    norm_gain,
    head_weight,
    targets,
):
    groups = lax.axis_size("req")
    req_index = lax.axis_index("req")
    fresh_count = queries.shape[0]
    kv_heads = scored_key_value.shape[2] // HEAD_SIZE
    queries_per_group = queries.shape[1] // scored_key_value.shape[2]
    page_len = page_kv.shape[2]
    store_pages = page_kv.shape[1]
    page_slots = page_table.shape[1]
    score_scale = HEAD_SIZE ** (-0.5)
    indices = jnp.arange(groups, dtype=jnp.int32)
    holder = jnp.sum(
        jnp.where(assignment[:, None] == indices[None, :], indices[:, None], 0), axis=0
    )
    query_heads = queries.reshape(fresh_count, kv_heads, queries_per_group, HEAD_SIZE)
    scored_keys = scored_key_value[0].reshape(fresh_count, kv_heads, HEAD_SIZE)
    scored_values = scored_key_value[1].reshape(fresh_count, kv_heads, HEAD_SIZE)
    fresh_order = offsets[0]
    visible = fresh_order[None, :] <= fresh_order[:, None]
    fresh_scores = (
        jnp.einsum("tjgd,ujd->jgtu", query_heads, scored_keys, preferred_element_type=jnp.float32)
        * score_scale
    )
    fresh_scores = jnp.where(visible[None, None], fresh_scores, FLOOR_SCORE)
    fresh_top = jnp.max(fresh_scores, axis=-1)
    fresh_weights = jnp.exp(fresh_scores - fresh_top[..., None])
    fresh_sum = jnp.sum(fresh_weights, axis=-1)
    fresh_acc = jnp.einsum(
        "jgtu,ujd->jgtd",
        fresh_weights.astype(jnp.bfloat16),
        scored_values,
        preferred_element_type=jnp.float32,
    )
    all_queries = lax.all_to_all(
        jnp.broadcast_to(query_heads[None], (groups,) + query_heads.shape), "req", 0, 0, tiled=True
    )
    page_owner = jnp.where(page_table >= 0, page_table // store_pages, -1)
    page_slot = page_table % store_pages
    is_mine = page_owner == req_index
    page_rank = jnp.cumsum(is_mine.astype(jnp.int32), axis=1) - 1
    page_fill = jnp.clip(
        lengths[:, None] - jnp.arange(page_slots, dtype=jnp.int32)[None, :] * page_len, 0, page_len
    )
    slot_picks = [
        jnp.sum(jnp.where(is_mine & (page_rank == cap_index), page_slot, 0), axis=1)
        for cap_index in range(CAP)
    ]
    fill_picks = [
        jnp.sum(jnp.where(is_mine & (page_rank == cap_index), page_fill, 0), axis=1)
        for cap_index in range(CAP)
    ]
    send_slot = jnp.take(jnp.stack(slot_picks, axis=1), holder, axis=0).reshape(-1)
    send_fill = jnp.take(jnp.stack(fill_picks, axis=1), holder, axis=0)
    outgoing = jnp.take(page_kv, send_slot, axis=1, mode="clip").reshape(
        2, groups, CAP * page_len, kv_heads, HEAD_SIZE
    )
    live_keys = (
        jnp.arange(page_len, dtype=jnp.int32)[None, None, :] < send_fill[:, :, None]
    ).reshape(groups, CAP * page_len)
    scores = (
        jnp.einsum(
            "btjgd,bljd->bjgtl", all_queries, outgoing[0], preferred_element_type=jnp.float32
        )
        * score_scale
    )
    live = live_keys[:, None, None, None, :]
    scores = jnp.where(live, scores, FLOOR_SCORE)
    part_top = lax.reduce_precision(jnp.max(scores, axis=-1), exponent_bits=8, mantissa_bits=7)
    weights = jnp.where(live, jnp.exp(scores - part_top[..., None]), 0.0)
    part_sum = jnp.sum(weights, axis=-1)
    part_acc = jnp.einsum(
        "bjgtl,bljd->bjgtd",
        weights.astype(jnp.bfloat16),
        outgoing[1],
        preferred_element_type=jnp.float32,
    )
    sum_high = lax.reduce_precision(part_sum, exponent_bits=8, mantissa_bits=7)
    sum_rest = part_sum - sum_high
    sum_mid = lax.reduce_precision(sum_rest, exponent_bits=8, mantissa_bits=7)
    sum_low = sum_rest - sum_mid
    lanes = part_acc.shape[-1]
    pad = ((0, 0),) * 3 + ((0, lanes - fresh_count),)
    payload = jnp.concatenate(
        [part_acc]
        + [jnp.pad(v, pad)[..., None, :] for v in (part_top, sum_high, sum_mid, sum_low)],
        axis=3,
    ).astype(jnp.bfloat16)
    arrived = lax.all_to_all(payload, "req", 0, 0, tiled=True).astype(jnp.float32)
    arrived_acc = arrived[:, :, :, :fresh_count, :]
    arrived_top = arrived[:, :, :, fresh_count, :fresh_count]
    arrived_sum = (
        arrived[:, :, :, fresh_count + 1, :fresh_count]
        + arrived[:, :, :, fresh_count + 2, :fresh_count]
    ) + arrived[:, :, :, fresh_count + 3, :fresh_count]
    row_top = jnp.maximum(jnp.max(arrived_top, axis=0), fresh_top)
    arrived_scale = jnp.exp(arrived_top - row_top[None])
    fresh_scale = jnp.exp(fresh_top - row_top)
    weight_sum = jnp.sum(arrived_sum * arrived_scale, axis=0) + fresh_sum * fresh_scale
    summed = (
        jnp.sum(arrived_acc * arrived_scale[..., None], axis=0)
        + fresh_acc * fresh_scale[..., None]
    )
    attended = jnp.transpose(summed / weight_sum[..., None], (2, 0, 1, 3))
    gated_out = (
        attended.reshape(fresh_count, -1) * jax.nn.sigmoid(gate_logits.astype(jnp.float32))
    ).astype(jnp.bfloat16)
    update = jnp.dot(gated_out, out_weight, preferred_element_type=jnp.float32)
    mdl_size = lax.axis_size("mdl")
    mdl_index = lax.axis_index("mdl")
    share = fresh_count // mdl_size
    terms = lax.all_to_all(
        update.reshape(mdl_size, share, update.shape[1]), "mdl", 0, 0, tiled=True
    )
    row_update = terms[0]
    for member in range(1, mdl_size):
        row_update = row_update + terms[member]
    stream = (
        lax.dynamic_slice_in_dim(residual, mdl_index * share, share, 0).astype(jnp.float32)
        + row_update
    )
    normed_rows = (
        stream
        * lax.rsqrt(jnp.mean(stream * stream, axis=-1, keepdims=True) + NORM_EPSILON)
        * norm_gain.astype(jnp.float32)
    ).astype(jnp.bfloat16)
    normed = lax.all_to_all(
        jnp.broadcast_to(normed_rows[None], (mdl_size,) + normed_rows.shape), "mdl", 0, 0, tiled=True
    ).reshape(fresh_count, normed_rows.shape[1])
    logits = jnp.dot(
        lax.all_gather(normed, "req", axis=0, tiled=True),
        head_weight,
        preferred_element_type=jnp.float32,
    )
    vocab_width = head_weight.shape[1]
    mdl_index = lax.axis_index("mdl")
    vocab_start = (req_index * mdl_size + mdl_index) * vocab_width
    columns = vocab_start + jnp.arange(vocab_width, dtype=jnp.int32)
    chosen = jnp.sum(jnp.where(targets[:, None] == columns[None, :], logits, 0.0), axis=1)
    local_peak = jnp.max(logits, axis=1)
    local_weights = jnp.exp(logits - local_peak[:, None])
    stats = jnp.stack(
        [
            local_peak,
            jnp.sum(local_weights, axis=1),
            jnp.sum(local_weights * logits, axis=1),
            chosen,
        ],
        axis=1,
    ).reshape(groups, fresh_count, 4)
    stats = lax.all_to_all(stats, "req", 0, 0, tiled=True)
    stats = merge_stats(stats)
    stats = merge_stats(
        lax.all_to_all(jnp.broadcast_to(stats[None], (mdl_size,) + stats.shape), "mdl", 0, 0, tiled=True)
    )
    row_peak, vocab_total, moment, chosen = (stats[:, i] for i in range(4))
    log_total = row_peak + jnp.log(vocab_total)
    logprob = chosen - log_total
    entropy = log_total - moment / vocab_total
    return (logprob, entropy)


def solution(mesh):
    placed = (
        P("req", "mdl"),
        P(None, "req", "mdl"),
        P("req", "mdl"),
        P(None, "req", None, "mdl"),
        P(),
        P(),
        P(),
        P("req", None),
        P("req", None),
        P("mdl", None),
        P(),
        P(None, ("req", "mdl")),
        P(),
    )
    return jax.shard_map(
        body, mesh=mesh, in_specs=placed, out_specs=(P("req"), P("req")), check_vma=False
    )
```

```python
import jax
import jax.numpy as jnp
from jax import lax
from jax.sharding import PartitionSpec as P

HEAD_SIZE = 128
CAP = 2


FLOOR_SCORE = -1e30
NORM_EPSILON = 1e-06


def merge_stats(parts):
    peak = jnp.max(parts[:, :, 0], axis=0)
    scale = jnp.exp(parts[:, :, 0] - peak[None])
    total = jnp.sum(parts[:, :, 1] * scale, axis=0)
    moment = jnp.sum(parts[:, :, 2] * scale, axis=0)
    chosen = jnp.sum(parts[:, :, 3], axis=0)
    return jnp.stack([peak, total, moment, chosen], axis=1)


def body(
    queries,
    scored_key_value,
    gate_logits,
    page_kv,
    page_table,
    lengths,
    assignment,
    offsets,
    residual,
    out_weight,
    norm_gain,
    head_weight,
    targets,
):
    groups = lax.axis_size("req")
    req_index = lax.axis_index("req")
    fresh_count = queries.shape[0]
    kv_heads = scored_key_value.shape[2] // HEAD_SIZE
    queries_per_group = queries.shape[1] // scored_key_value.shape[2]
    page_len = page_kv.shape[2]
    store_pages = page_kv.shape[1]
    page_slots = page_table.shape[1]
    score_scale = HEAD_SIZE ** (-0.5)
    indices = jnp.arange(groups, dtype=jnp.int32)
    holder = jnp.sum(
        jnp.where(assignment[:, None] == indices[None, :], indices[:, None], 0), axis=0
    )
    query_heads = queries.reshape(fresh_count, kv_heads, queries_per_group, HEAD_SIZE)
    scored_keys = scored_key_value[0].reshape(fresh_count, kv_heads, HEAD_SIZE)
    scored_values = scored_key_value[1].reshape(fresh_count, kv_heads, HEAD_SIZE)
    fresh_order = offsets[0]
    visible = fresh_order[None, :] <= fresh_order[:, None]
    fresh_scores = (
        jnp.einsum("tjgd,ujd->jgtu", query_heads, scored_keys, preferred_element_type=jnp.float32)
        * score_scale
    )
    fresh_scores = jnp.where(visible[None, None], fresh_scores, FLOOR_SCORE)
    fresh_top = jnp.max(fresh_scores, axis=-1)
    fresh_weights = jnp.exp(fresh_scores - fresh_top[..., None])
    fresh_sum = jnp.sum(fresh_weights, axis=-1)
    fresh_acc = jnp.einsum(
        "jgtu,ujd->jgtd",
        fresh_weights.astype(jnp.bfloat16),
        scored_values,
        preferred_element_type=jnp.float32,
    )
    all_queries = lax.all_to_all(
        jnp.broadcast_to(query_heads[None], (groups,) + query_heads.shape), "req", 0, 0, tiled=True
    )
    page_owner = jnp.where(page_table >= 0, page_table // store_pages, -1)
    page_slot = page_table % store_pages
    is_mine = page_owner == req_index
    page_rank = jnp.cumsum(is_mine.astype(jnp.int32), axis=1) - 1
    page_fill = jnp.clip(
        lengths[:, None] - jnp.arange(page_slots, dtype=jnp.int32)[None, :] * page_len, 0, page_len
    )
    slot_picks = [
        jnp.sum(jnp.where(is_mine & (page_rank == cap_index), page_slot, 0), axis=1)
        for cap_index in range(CAP)
    ]
    fill_picks = [
        jnp.sum(jnp.where(is_mine & (page_rank == cap_index), page_fill, 0), axis=1)
        for cap_index in range(CAP)
    ]
    send_slot = jnp.take(jnp.stack(slot_picks, axis=1), holder, axis=0).reshape(-1)
    send_fill = jnp.take(jnp.stack(fill_picks, axis=1), holder, axis=0)
    stored = req_index * store_pages + jnp.arange(store_pages, dtype=jnp.int32)
    match = page_table[None, :, :] == stored[:, None, None]
    slot_used = jnp.any(match, axis=(1, 2))
    slot_request = jnp.sum(jnp.where(match, indices[None, :, None], 0), axis=(1, 2))
    slot_position = jnp.sum(
        jnp.where(match, jnp.arange(page_slots, dtype=jnp.int32)[None, None, :], 0), axis=(1, 2)
    )
    slot_fill = jnp.where(
        slot_used,
        jnp.clip(
            jnp.take(lengths, slot_request, mode="clip") - slot_position * page_len, 0, page_len
        ),
        0,
    )
    slot_dest = jnp.take(assignment, slot_request, mode="clip")
    slot_queries = jnp.take(all_queries, slot_dest, axis=0, mode="clip")
    slot_keys = page_kv[0].reshape(store_pages, page_len, kv_heads, HEAD_SIZE)
    slot_values = page_kv[1].reshape(store_pages, page_len, kv_heads, HEAD_SIZE)
    slot_live = (jnp.arange(page_len, dtype=jnp.int32)[None, :] < slot_fill[:, None])[
        :, None, None, None, :
    ]
    slot_scores = (
        jnp.einsum(
            "stjgd,sljd->sjgtl", slot_queries, slot_keys, preferred_element_type=jnp.float32
        )
        * score_scale
    )
    slot_scores = jnp.where(slot_live, slot_scores, FLOOR_SCORE)
    slot_top = lax.reduce_precision(
        jnp.max(slot_scores, axis=-1), exponent_bits=8, mantissa_bits=7
    )
    slot_weights = jnp.where(slot_live, jnp.exp(slot_scores - slot_top[..., None]), 0.0)
    slot_sum = jnp.sum(slot_weights, axis=-1)
    slot_acc = jnp.einsum(
        "sjgtl,sljd->sjgtd",
        slot_weights.astype(jnp.bfloat16),
        slot_values,
        preferred_element_type=jnp.float32,
    )
    present = (send_fill > 0).reshape(-1)
    bucket = (groups, CAP) + slot_top.shape[1:]
    cap_top = jnp.where(
        present[:, None, None, None], jnp.take(slot_top, send_slot, axis=0, mode="clip"), FLOOR_SCORE
    ).reshape(bucket)
    cap_sum = jnp.where(
        present[:, None, None, None], jnp.take(slot_sum, send_slot, axis=0, mode="clip"), 0.0
    ).reshape(bucket)
    cap_acc = jnp.where(
        present[:, None, None, None, None], jnp.take(slot_acc, send_slot, axis=0, mode="clip"), 0.0
    ).reshape(bucket + (HEAD_SIZE,))
    part_top = jnp.max(cap_top, axis=1)
    cap_scale = jnp.exp(cap_top - part_top[:, None])
    part_sum = jnp.sum(cap_sum * cap_scale, axis=1)
    part_acc = jnp.sum(cap_acc * cap_scale[..., None], axis=1)
    sum_high = lax.reduce_precision(part_sum, exponent_bits=8, mantissa_bits=7)
    sum_rest = part_sum - sum_high
    sum_mid = lax.reduce_precision(sum_rest, exponent_bits=8, mantissa_bits=7)
    sum_low = sum_rest - sum_mid
    lanes = part_acc.shape[-1]
    pad = ((0, 0),) * 3 + ((0, lanes - fresh_count),)
    payload = jnp.concatenate(
        [part_acc]
        + [jnp.pad(v, pad)[..., None, :] for v in (part_top, sum_high, sum_mid, sum_low)],
        axis=3,
    ).astype(jnp.bfloat16)
    arrived = lax.all_to_all(payload, "req", 0, 0, tiled=True).astype(jnp.float32)
    arrived_acc = arrived[:, :, :, :fresh_count, :]
    arrived_top = arrived[:, :, :, fresh_count, :fresh_count]
    arrived_sum = (
        arrived[:, :, :, fresh_count + 1, :fresh_count]
        + arrived[:, :, :, fresh_count + 2, :fresh_count]
    ) + arrived[:, :, :, fresh_count + 3, :fresh_count]
    row_top = jnp.maximum(jnp.max(arrived_top, axis=0), fresh_top)
    arrived_scale = jnp.exp(arrived_top - row_top[None])
    fresh_scale = jnp.exp(fresh_top - row_top)
    weight_sum = jnp.sum(arrived_sum * arrived_scale, axis=0) + fresh_sum * fresh_scale
    summed = (
        jnp.sum(arrived_acc * arrived_scale[..., None], axis=0)
        + fresh_acc * fresh_scale[..., None]
    )
    attended = jnp.transpose(summed / weight_sum[..., None], (2, 0, 1, 3))
    gated_out = (
        attended.reshape(fresh_count, -1) * jax.nn.sigmoid(gate_logits.astype(jnp.float32))
    ).astype(jnp.bfloat16)
    update = jnp.dot(gated_out, out_weight, preferred_element_type=jnp.float32)
    mdl_size = lax.axis_size("mdl")
    mdl_index = lax.axis_index("mdl")
    share = fresh_count // mdl_size
    terms = lax.all_to_all(
        update.reshape(mdl_size, share, update.shape[1]), "mdl", 0, 0, tiled=True
    )
    row_update = terms[0]
    for member in range(1, mdl_size):
        row_update = row_update + terms[member]
    stream = (
        lax.dynamic_slice_in_dim(residual, mdl_index * share, share, 0).astype(jnp.float32)
        + row_update
    )
    normed_rows = (
        stream
        * lax.rsqrt(jnp.mean(stream * stream, axis=-1, keepdims=True) + NORM_EPSILON)
        * norm_gain.astype(jnp.float32)
    ).astype(jnp.bfloat16)
    normed = lax.all_to_all(
        jnp.broadcast_to(normed_rows[None], (mdl_size,) + normed_rows.shape), "mdl", 0, 0, tiled=True
    ).reshape(fresh_count, normed_rows.shape[1])
    logits = jnp.dot(
        lax.all_gather(normed, "req", axis=0, tiled=True),
        head_weight,
        preferred_element_type=jnp.float32,
    )
    vocab_width = head_weight.shape[1]
    mdl_index = lax.axis_index("mdl")
    vocab_start = (req_index * mdl_size + mdl_index) * vocab_width
    columns = vocab_start + jnp.arange(vocab_width, dtype=jnp.int32)
    chosen = jnp.sum(jnp.where(targets[:, None] == columns[None, :], logits, 0.0), axis=1)
    local_peak = jnp.max(logits, axis=1)
    local_weights = jnp.exp(logits - local_peak[:, None])
    stats = jnp.stack(
        [
            local_peak,
            jnp.sum(local_weights, axis=1),
            jnp.sum(local_weights * logits, axis=1),
            chosen,
        ],
        axis=1,
    ).reshape(groups, fresh_count, 4)
    stats = lax.all_to_all(stats, "req", 0, 0, tiled=True)
    stats = merge_stats(stats)
    stats = merge_stats(
        lax.all_to_all(jnp.broadcast_to(stats[None], (mdl_size,) + stats.shape), "mdl", 0, 0, tiled=True)
    )
    row_peak, vocab_total, moment, chosen = (stats[:, i] for i in range(4))
    log_total = row_peak + jnp.log(vocab_total)
    logprob = chosen - log_total
    entropy = log_total - moment / vocab_total
    return (logprob, entropy)


def solution(mesh):
    placed = (
        P("req", "mdl"),
        P(None, "req", "mdl"),
        P("req", "mdl"),
        P(None, "req", None, "mdl"),
        P(),
        P(),
        P(),
        P("req", None),
        P("req", None),
        P("mdl", None),
        P(),
        P(None, ("req", "mdl")),
        P(),
    )
    return jax.shard_map(
        body, mesh=mesh, in_specs=placed, out_specs=(P("req"), P("req")), check_vma=False
    )
```

```python
import jax
import jax.numpy as jnp
from jax import lax
from jax.sharding import PartitionSpec as P

HEAD_SIZE = 128
CAP = 2


FLOOR_SCORE = -1e30
NORM_EPSILON = 1e-06


def merge_stats(parts):
    peak = jnp.max(parts[:, :, 0], axis=0)
    scale = jnp.exp(parts[:, :, 0] - peak[None])
    total = jnp.sum(parts[:, :, 1] * scale, axis=0)
    moment = jnp.sum(parts[:, :, 2] * scale, axis=0)
    chosen = jnp.sum(parts[:, :, 3], axis=0)
    return jnp.stack([peak, total, moment, chosen], axis=1)


def body(
    queries,
    scored_key_value,
    gate_logits,
    page_kv,
    page_table,
    lengths,
    assignment,
    offsets,
    residual,
    out_weight,
    norm_gain,
    head_weight,
    targets,
):
    groups = lax.axis_size("req")
    req_index = lax.axis_index("req")
    fresh_count = queries.shape[0]
    kv_heads = scored_key_value.shape[2] // HEAD_SIZE
    queries_per_group = queries.shape[1] // scored_key_value.shape[2]
    page_len = page_kv.shape[2]
    store_pages = page_kv.shape[1]
    page_slots = page_table.shape[1]
    score_scale = HEAD_SIZE ** (-0.5)
    indices = jnp.arange(groups, dtype=jnp.int32)
    holder = jnp.sum(
        jnp.where(assignment[:, None] == indices[None, :], indices[:, None], 0), axis=0
    )
    query_heads = queries.reshape(fresh_count, kv_heads, queries_per_group, HEAD_SIZE)
    scored_keys = scored_key_value[0].reshape(fresh_count, kv_heads, HEAD_SIZE)
    scored_values = scored_key_value[1].reshape(fresh_count, kv_heads, HEAD_SIZE)
    fresh_order = offsets[0]
    visible = fresh_order[None, :] <= fresh_order[:, None]
    fresh_scores = (
        jnp.einsum("tjgd,ujd->jgtu", query_heads, scored_keys, preferred_element_type=jnp.float32)
        * score_scale
    )
    fresh_scores = jnp.where(visible[None, None], fresh_scores, FLOOR_SCORE)
    fresh_top = jnp.max(fresh_scores, axis=-1)
    fresh_weights = jnp.exp(fresh_scores - fresh_top[..., None])
    fresh_sum = jnp.sum(fresh_weights, axis=-1)
    fresh_acc = jnp.einsum(
        "jgtu,ujd->jgtd",
        fresh_weights.astype(jnp.bfloat16),
        scored_values,
        preferred_element_type=jnp.float32,
    )
    all_queries = lax.all_to_all(
        jnp.broadcast_to(query_heads[None], (groups,) + query_heads.shape), "req", 0, 0, tiled=True
    )
    page_owner = jnp.where(page_table >= 0, page_table // store_pages, -1)
    page_slot = page_table % store_pages
    is_mine = page_owner == req_index
    page_rank = jnp.cumsum(is_mine.astype(jnp.int32), axis=1) - 1
    page_fill = jnp.clip(
        lengths[:, None] - jnp.arange(page_slots, dtype=jnp.int32)[None, :] * page_len, 0, page_len
    )
    slot_picks = [
        jnp.sum(jnp.where(is_mine & (page_rank == cap_index), page_slot, 0), axis=1)
        for cap_index in range(CAP)
    ]
    fill_picks = [
        jnp.sum(jnp.where(is_mine & (page_rank == cap_index), page_fill, 0), axis=1)
        for cap_index in range(CAP)
    ]
    send_slot = jnp.take(jnp.stack(slot_picks, axis=1), holder, axis=0).reshape(-1)
    send_fill = jnp.take(jnp.stack(fill_picks, axis=1), holder, axis=0)
    stored = req_index * store_pages + jnp.arange(store_pages, dtype=jnp.int32)
    match = page_table[None, :, :] == stored[:, None, None]
    slot_used = jnp.any(match, axis=(1, 2))
    slot_request = jnp.sum(jnp.where(match, indices[None, :, None], 0), axis=(1, 2))
    slot_position = jnp.sum(
        jnp.where(match, jnp.arange(page_slots, dtype=jnp.int32)[None, None, :], 0), axis=(1, 2)
    )
    slot_fill = jnp.where(
        slot_used,
        jnp.clip(
            jnp.take(lengths, slot_request, mode="clip") - slot_position * page_len, 0, page_len
        ),
        0,
    )
    slot_dest = jnp.take(assignment, slot_request, mode="clip")
    slot_queries = jnp.take(all_queries, slot_dest, axis=0, mode="clip")
    slot_keys = page_kv[0].reshape(store_pages, page_len, kv_heads, HEAD_SIZE)
    slot_values = page_kv[1].reshape(store_pages, page_len, kv_heads, HEAD_SIZE)
    slot_live = (jnp.arange(page_len, dtype=jnp.int32)[None, :] < slot_fill[:, None])[
        :, None, None, None, :
    ]
    slot_scores = (
        jnp.einsum(
            "stjgd,sljd->sjgtl", slot_queries, slot_keys, preferred_element_type=jnp.float32
        )
        * score_scale
    )
    slot_scores = jnp.where(slot_live, slot_scores, FLOOR_SCORE)
    slot_top = lax.reduce_precision(
        jnp.max(slot_scores, axis=-1), exponent_bits=8, mantissa_bits=7
    )
    slot_weights = jnp.where(slot_live, jnp.exp(slot_scores - slot_top[..., None]), 0.0)
    slot_sum = jnp.sum(slot_weights, axis=-1)
    slot_acc = jnp.einsum(
        "sjgtl,sljd->sjgtd",
        slot_weights.astype(jnp.bfloat16),
        slot_values,
        preferred_element_type=jnp.float32,
    )
    present = (send_fill > 0).reshape(-1)
    bucket = (groups, CAP) + slot_top.shape[1:]
    cap_top = jnp.where(
        present[:, None, None, None], jnp.take(slot_top, send_slot, axis=0, mode="clip"), FLOOR_SCORE
    ).reshape(bucket)
    cap_sum = jnp.where(
        present[:, None, None, None], jnp.take(slot_sum, send_slot, axis=0, mode="clip"), 0.0
    ).reshape(bucket)
    cap_acc = jnp.where(
        present[:, None, None, None, None], jnp.take(slot_acc, send_slot, axis=0, mode="clip"), 0.0
    ).reshape(bucket + (HEAD_SIZE,))
    part_top = jnp.max(cap_top, axis=1)
    cap_scale = jnp.exp(cap_top - part_top[:, None])
    part_sum = jnp.sum(cap_sum * cap_scale, axis=1)
    part_acc = jnp.sum(cap_acc * cap_scale[..., None], axis=1)
    sum_high = lax.reduce_precision(part_sum, exponent_bits=8, mantissa_bits=7)
    sum_rest = part_sum - sum_high
    sum_mid = lax.reduce_precision(sum_rest, exponent_bits=8, mantissa_bits=7)
    sum_low = sum_rest - sum_mid
    lanes = part_acc.shape[-1]
    pad = ((0, 0),) * 3 + ((0, lanes - fresh_count),)
    payload = jnp.concatenate(
        [part_acc]
        + [jnp.pad(v, pad)[..., None, :] for v in (part_top, sum_high, sum_mid, sum_low)],
        axis=3,
    ).astype(jnp.bfloat16)
    arrived = lax.all_to_all(payload, "req", 0, 0, tiled=True)
    arrived_acc = arrived[:, :, :, :fresh_count, :].astype(jnp.float32)
    arrived_rows = arrived[:, :, :, fresh_count:, :fresh_count].astype(jnp.float32)
    arrived_top = arrived_rows[:, :, :, 0]
    arrived_sum = (arrived_rows[:, :, :, 1] + arrived_rows[:, :, :, 2]) + arrived_rows[:, :, :, 3]
    row_top = jnp.maximum(jnp.max(arrived_top, axis=0), fresh_top)
    arrived_scale = jnp.exp(arrived_top - row_top[None])
    fresh_scale = jnp.exp(fresh_top - row_top)
    weight_sum = jnp.sum(arrived_sum * arrived_scale, axis=0) + fresh_sum * fresh_scale
    summed = (
        jnp.sum(arrived_acc * arrived_scale[..., None], axis=0)
        + fresh_acc * fresh_scale[..., None]
    )
    attended = jnp.transpose(summed / weight_sum[..., None], (2, 0, 1, 3))
    gated_out = (
        attended.reshape(fresh_count, -1) * jax.nn.sigmoid(gate_logits.astype(jnp.float32))
    ).astype(jnp.bfloat16)
    update = jnp.dot(gated_out, out_weight, preferred_element_type=jnp.float32)
    mdl_size = lax.axis_size("mdl")
    mdl_index = lax.axis_index("mdl")
    share = fresh_count // mdl_size
    terms = lax.all_to_all(
        update.reshape(mdl_size, share, update.shape[1]), "mdl", 0, 0, tiled=True
    )
    row_update = terms[0]
    for member in range(1, mdl_size):
        row_update = row_update + terms[member]
    stream = (
        lax.dynamic_slice_in_dim(residual, mdl_index * share, share, 0).astype(jnp.float32)
        + row_update
    )
    normed_rows = (
        stream
        * lax.rsqrt(jnp.mean(stream * stream, axis=-1, keepdims=True) + NORM_EPSILON)
        * norm_gain.astype(jnp.float32)
    ).astype(jnp.bfloat16)
    normed = lax.all_to_all(
        jnp.broadcast_to(normed_rows[None], (mdl_size,) + normed_rows.shape), "mdl", 0, 0, tiled=True
    ).reshape(fresh_count, normed_rows.shape[1])
    logits = jnp.dot(
        lax.all_gather(normed, "req", axis=0, tiled=True),
        head_weight,
        preferred_element_type=jnp.float32,
    )
    vocab_width = head_weight.shape[1]
    mdl_index = lax.axis_index("mdl")
    vocab_start = (req_index * mdl_size + mdl_index) * vocab_width
    columns = vocab_start + jnp.arange(vocab_width, dtype=jnp.int32)
    chosen = jnp.sum(jnp.where(targets[:, None] == columns[None, :], logits, 0.0), axis=1)
    local_peak = jnp.max(logits, axis=1)
    local_weights = jnp.exp(logits - local_peak[:, None])
    stats = jnp.stack(
        [
            local_peak,
            jnp.sum(local_weights, axis=1),
            jnp.sum(local_weights * logits, axis=1),
            chosen,
        ],
        axis=1,
    ).reshape(groups, fresh_count, 4)
    stats = lax.all_to_all(stats, "req", 0, 0, tiled=True)
    stats = merge_stats(stats)
    stats = merge_stats(
        lax.all_to_all(jnp.broadcast_to(stats[None], (mdl_size,) + stats.shape), "mdl", 0, 0, tiled=True)
    )
    row_peak, vocab_total, moment, chosen = (stats[:, i] for i in range(4))
    log_total = row_peak + jnp.log(vocab_total)
    logprob = chosen - log_total
    entropy = log_total - moment / vocab_total
    return (logprob, entropy)


def solution(mesh):
    placed = (
        P("req", "mdl"),
        P(None, "req", "mdl"),
        P("req", "mdl"),
        P(None, "req", None, "mdl"),
        P(),
        P(),
        P(),
        P("req", None),
        P("req", None),
        P("mdl", None),
        P(),
        P(None, ("req", "mdl")),
        P(),
    )
    return jax.shard_map(
        body, mesh=mesh, in_specs=placed, out_specs=(P("req"), P("req")), check_vma=False
    )
```
